128 devices in a mesh: gx: 16 (over z, x), gy: 8 (over y, core).
Axes of the slice: x: 4, y: 4, z: 4, core: 2. Of those that a mesh axis runs over, the one named last changes fastest.
Arguments:
- tokens: bfloat16 [2048, 8192], P('gy', 'gx'), may hold values from -6 to 6
- gate_base_weight: bfloat16 [8192, 29568], P('gx', 'gy'), may hold values from -0.0625 to 0.0625
- up_base_weight: bfloat16 [8192, 29568], P('gx', 'gy'), may hold values from -0.0625 to 0.0625
- adapter_down_maps: bfloat16 [128, 8192, 128], P(('gx', 'gy')), may hold values from -0.0625 to 0.0625
- adapter_up_maps: bfloat16 [128, 128, 29568], P(('gx', 'gy')), may hold values from -0.75 to 0.75
- tenant: int32 [2048, 1], replicated, may hold values from 0 to 127; in each aligned block of 128 rows (0 to 127, 128 to 255, ...) at most 4 rows name the same one
- tenant_slot_index: int32 [128], replicated, may hold values from 0 to 127, as said below
Outputs:
- hidden: bfloat16 [2048, 29568], P('gx', 'gy')
The draws below stay inside these ranges and needn't reach their ends.
Inputs may be any that keep to these rules, and one draw needn't show every extreme that they name: In each aligned block of 128 rows no tenant names more than 4 rows, and in some block a tenant names exactly 4. `tenant_slot_index`: A permutation of the slots; slot s is held by device s of gx+gy, gx the slower index.
All inputs are finite; a program needn't handle non-finite values.
Results may differ from the reference program's by a relative error of at most 0.019.
Values may be sent and summed in bfloat16 or wider, within the bound.
No kernel may reach another device: no remote copies, remote signals or barrier semaphores. Data moves between devices by JAX's collectives and lax.ppermute only.
A program may use at most 192 MiB of HBM per device.

```python
import math
import jax
import jax.numpy as jnp
import numpy as np
from jax import lax

MODEL_WIDTH = 8192
HIDDEN_UNITS = 29568
ADAPTER_RANK = 64
BLK = 128
CAP = 4
ROWS = 2048
TENANT_COUNT = 128
N_GX = 16


def draw_tenant_slot_index(key, part):
    return jax.random.permutation(jax.random.fold_in(key, 7), TENANT_COUNT).astype(jnp.int32)


def levels(rng, dims, cuts, least, largest):
    loudness, own = 1.0, jax.random.fold_in(rng, 6)
    for position, shards_of in cuts:
        steps = jnp.exp(jax.random.uniform(jax.random.fold_in(own, position), (shards_of,), jnp.float32, least / len(cuts), largest / len(cuts)))
        loudness = loudness * jnp.repeat(steps, dims[position] // shards_of).reshape([-1 if axis == position else 1 for axis in range(len(dims))])
    return loudness


def assign_block(key, own, number, rows, amount, top, limit, lean):
    order = jax.random.permutation(key, amount)
    packed, usual = load_shares(amount, rows * top, limit, lean, True), load_shares(amount, rows * top, limit, lean, False)
    places = jnp.arange(amount)

    def named(lengths, turn):
        used = int((lengths > 0).sum())
        fixed = max(1, used // 4)
        shifted = fixed + (places - fixed + turn * (used - fixed)) % max(1, amount - fixed)
        return jnp.zeros((amount,), jnp.int32).at[order[jnp.where(places < fixed, places, shifted)]].set(jnp.asarray(lengths, jnp.int32))

    lengths = jnp.where(number % 4 == 0, named(packed, number // 4), named(usual, number - number // 4 - 1))
    mixed = jax.random.permutation(jax.random.fold_in(own, 3), amount)
    source_of, sink = mixed[0:amount // 2 * 2:2], mixed[1:amount // 2 * 2:2]
    room = jnp.minimum(lengths[source_of] - 1, limit - lengths[sink]) // 2
    room = jnp.where((source_of == order[0]) | (sink == order[0]) | (lengths[sink] == 0), 0, jnp.maximum(room, 0))
    shifted = jax.random.randint(jax.random.fold_in(own, 4), (amount // 2,), 0, 1 << 20) % (room + 1)
    lengths = lengths.at[source_of].add(-shifted).at[sink].add(shifted)
    members = jnp.searchsorted(jnp.cumsum(lengths), jnp.arange(rows * top), side="right").astype(jnp.int32)
    table = members.reshape(top, rows).T
    table = table[jax.random.permutation(jax.random.fold_in(own, 1), rows)]
    turn = jax.random.randint(jax.random.fold_in(own, 2), (rows, 1), 0, top)
    return jnp.take_along_axis(table, (jnp.arange(top)[None, :] + turn) % top, axis=1)


def load_shares(count, total, bound, lean, full):
    loads = [(1 << 20) // math.isqrt(rank ** lean) + 1 for rank in range(1, count + 1)]
    largest = bound if full else min(bound, max(-(-total // count), total * loads[0] // sum(loads)))
    least = 1 if total - largest >= count - 1 else 0
    holding, surplus = [largest] + [least] * (count - 1), total - largest - least * (count - 1)
    while surplus > 0:
        movable = [i for i in range(1, count) if holding[i] < largest] or [i for i in range(1, count) if holding[i] < bound]
        whole, left = sum([loads[i] for i in movable]), surplus
        for i in movable:
            more = min(bound - holding[i], max(1, left * loads[i] // whole), surplus)
            holding[i] = holding[i] + more
            surplus = surplus - more
    return np.array(holding)


def noise(own_key, dims, scale, most, shards=(), kind=jnp.bfloat16):
    gain = levels(own_key, dims, shards, -0.22, 0.18) if shards else 1.0
    values = jax.random.normal(own_key, dims, jnp.float32) * scale * gain
    return jnp.minimum(jnp.maximum(values, -most), most).astype(kind)


def setup_inputs(seed: int = 0) -> dict:
    streams_of = jax.random.split(jax.random.key(seed), 8)
    tokens = noise(streams_of[0], (ROWS, MODEL_WIDTH), 1.0, 6.0, ((0, 8), (1, 16)))
    gate_base_weight = noise(streams_of[1], (MODEL_WIDTH, HIDDEN_UNITS), MODEL_WIDTH ** -0.5, 0.0625, ((0, 16), (1, 8)))
    up_base_weight = noise(streams_of[2], (MODEL_WIDTH, HIDDEN_UNITS), MODEL_WIDTH ** -0.5, 0.0625, ((0, 16), (1, 8)))
    adapter_down_maps = noise(streams_of[3], (TENANT_COUNT, MODEL_WIDTH, 2 * ADAPTER_RANK), MODEL_WIDTH ** -0.5, 0.0625, ((0, 128),))
    adapter_up_maps = noise(streams_of[4], (TENANT_COUNT, 2 * ADAPTER_RANK, HIDDEN_UNITS), ADAPTER_RANK ** -0.5, 0.75, ((0, 128),))
    tenant_keys = jax.random.split(jax.random.fold_in(streams_of[5], 1), ROWS // BLK)
    tenant_turns = jax.random.permutation(jax.random.fold_in(streams_of[5], 3), ROWS // BLK)
    tenant = jax.vmap(lambda own, number: assign_block(jax.random.fold_in(streams_of[5], 2), own, number, BLK, TENANT_COUNT, 1, CAP, 2))(tenant_keys, tenant_turns).reshape((ROWS, 1))
    tenant_slot_index = draw_tenant_slot_index(jax.random.fold_in(streams_of[7], 71), 0)
    return {"tokens": tokens, "gate_base_weight": gate_base_weight, "up_base_weight": up_base_weight, "adapter_down_maps": adapter_down_maps, "adapter_up_maps": adapter_up_maps, "tenant": tenant, "tenant_slot_index": tenant_slot_index}


def reference(tokens, gate_base_weight, up_base_weight, adapter_down_maps, adapter_up_maps, tenant, tenant_slot_index):
    tile_width = MODEL_WIDTH // N_GX

    def add_block(totals, block):
        start = (block * tile_width).astype(jnp.int32)
        rows = lax.dynamic_slice_in_dim(tokens, start, tile_width, 1)
        gate_rows = lax.dynamic_slice_in_dim(gate_base_weight, start, tile_width, 0)
        up_rows = lax.dynamic_slice_in_dim(up_base_weight, start, tile_width, 0)
        part_gate = lax.optimization_barrier(jnp.dot(rows, gate_rows, preferred_element_type=jnp.float32).astype(jnp.bfloat16))
        part_up = lax.optimization_barrier(jnp.dot(rows, up_rows, preferred_element_type=jnp.float32).astype(jnp.bfloat16))
        return (totals[0] + part_gate.astype(jnp.float32), totals[1] + part_up.astype(jnp.float32)), None

    zeros = jnp.zeros((ROWS, HIDDEN_UNITS), jnp.float32)
    (gate_base, up_base), _ = lax.scan(add_block, (zeros, zeros), jnp.arange(N_GX, dtype=jnp.int32))
    slots = tenant_slot_index[tenant[:, 0]].astype(jnp.int32)

    def adapt(item):
        row, adapter_slot = item
        down_matrix = lax.dynamic_index_in_dim(adapter_down_maps, adapter_slot, 0, keepdims=False)
        up_map_matrix = lax.dynamic_index_in_dim(adapter_up_maps, adapter_slot, 0, keepdims=False)
        low = jnp.dot(row[None, :], down_matrix, preferred_element_type=jnp.float32).astype(jnp.bfloat16)
        delta_gate = jnp.dot(low[:, :ADAPTER_RANK], up_map_matrix[:ADAPTER_RANK], preferred_element_type=jnp.float32).astype(jnp.bfloat16)
        delta_up = jnp.dot(low[:, ADAPTER_RANK:], up_map_matrix[ADAPTER_RANK:], preferred_element_type=jnp.float32).astype(jnp.bfloat16)
        return delta_gate[0], delta_up[0]

    delta_gate, delta_up = lax.map(adapt, (tokens, slots))
    gate = gate_base + delta_gate.astype(jnp.float32)
    up_value = up_base + delta_up.astype(jnp.float32)
    return (jax.nn.silu(gate) * up_value).astype(jnp.bfloat16)
```

```python
import jax
import jax.numpy as jnp
from jax import lax
from jax.sharding import PartitionSpec as P
from jax.experimental.layout import Layout, with_layout_constraint

CAP = 4


def body(
    tokens,
    gate_base_weight,
    up_base_weight,
    adapter_down_maps,
    adapter_up_maps,
    tenant,
    tenant_slot_index,
):
    tile_grid_rows = lax.axis_size("gx")
    tile_grid_columns = lax.axis_size("gy")
    devices = tile_grid_rows * tile_grid_columns
    row_gx = lax.axis_index("gx")
    row_gy = lax.axis_index("gy")
    local_rows = tokens.shape[0]
    tile_width = tokens.shape[1]
    total_rows = tenant.shape[0]
    block = total_rows // tile_grid_rows
    groups = local_rows // block
    tenants = tenant_slot_index.shape[0]
    column_count = gate_base_weight.shape[1]
    doubled_rank = adapter_down_maps.shape[2]
    adapter_rank_width = doubled_rank // 2
    gathered = lax.all_gather(tokens, "gy", axis=0, tiled=True)
    gate_sum = lax.psum_scatter(
        with_layout_constraint(jnp.dot(gathered, gate_base_weight, preferred_element_type=jnp.float32).astype(jnp.bfloat16), Layout(major_to_minor=(0, 1))),
        "gx", scatter_dimension=0, tiled=True).astype(jnp.float32)
    up_sum = lax.psum_scatter(
        with_layout_constraint(jnp.dot(gathered, up_base_weight, preferred_element_type=jnp.float32).astype(jnp.bfloat16), Layout(major_to_minor=(0, 1))),
        "gx", scatter_dimension=0, tiled=True).astype(jnp.float32)
    slot_all = jnp.sum(
        jnp.where(tenant == lax.iota(jnp.int32, tenants)[None, :], tenant_slot_index[None, :], 0),
        axis=1,
    )
    onehot = (slot_all[:, None] == lax.iota(jnp.int32, devices)[None, :]).astype(jnp.int32)
    blocked = onehot.reshape(tile_grid_rows, block, devices)
    before = jnp.cumsum(blocked, axis=1) - blocked
    position = jnp.sum(before * blocked, axis=2).reshape(total_rows)
    send_slot = lax.dynamic_slice_in_dim(slot_all, row_gy * local_rows, local_rows)
    send_rank = lax.dynamic_slice_in_dim(position, row_gy * local_rows, local_rows)
    target = (send_slot * groups + lax.iota(jnp.int32, local_rows) // block) * CAP + send_rank
    outgoing = jnp.zeros((devices * groups * CAP, tile_width), jnp.bfloat16).at[target].set(tokens)
    arrived = lax.all_to_all(
        outgoing.reshape(devices, groups * CAP, tile_width),
        ("gx", "gy"),
        split_axis=0,
        concat_axis=0,
        tiled=True,
    )
    arrived = arrived.reshape(tile_grid_rows, tile_grid_columns * groups * CAP, tile_width)
    down_local = adapter_down_maps[0].reshape(tile_grid_rows, tile_width, doubled_rank)
    low = jnp.einsum("isk,ikr->sr", arrived, down_local, preferred_element_type=jnp.float32).astype(
        jnp.bfloat16
    )
    low = low.reshape(tile_grid_rows, CAP, doubled_rank)
    gate_up_map = adapter_up_maps[0, :adapter_rank_width].reshape(
        adapter_rank_width, tile_grid_columns, column_count
    )
    up_up_map = adapter_up_maps[0, adapter_rank_width:].reshape(
        adapter_rank_width, tile_grid_columns, column_count
    )
    delta_gate = jnp.einsum(
        "gcr,rjf->gjcf",
        low[:, :, :adapter_rank_width],
        gate_up_map,
        preferred_element_type=jnp.float32,
    ).astype(jnp.bfloat16)
    delta_up = jnp.einsum(
        "gcr,rjf->gjcf",
        low[:, :, adapter_rank_width:],
        up_up_map,
        preferred_element_type=jnp.float32,
    ).astype(jnp.bfloat16)
    back_gate, back_up = (
        lax.all_to_all(
            delta_gate.reshape(devices, CAP, column_count),
            ("gx", "gy"),
            split_axis=0,
            concat_axis=0,
            tiled=True,
        ),
        lax.all_to_all(
            delta_up.reshape(devices, CAP, column_count),
            ("gx", "gy"),
            split_axis=0,
            concat_axis=0,
            tiled=True,
        ),
    )
    back_gate = back_gate.reshape(devices * CAP, column_count)
    back_up = back_up.reshape(devices * CAP, column_count)
    own_slot = lax.dynamic_slice_in_dim(slot_all, row_gx * block, block)
    own_rank = lax.dynamic_slice_in_dim(position, row_gx * block, block)
    pick = own_slot * CAP + own_rank
    gate_value = gate_sum + back_gate[pick].astype(jnp.float32)
    up_value = up_sum + back_up[pick].astype(jnp.float32)
    return (jax.nn.silu(gate_value) * up_value).astype(jnp.bfloat16)


def solution(mesh):
    return jax.shard_map(
        body,
        mesh=mesh,
        in_specs=(
            P("gy", "gx"),
            P("gx", "gy"),
            P("gx", "gy"),
            P(("gx", "gy"), None, None),
            P(("gx", "gy"), None, None),
            P(),
            P(),
        ),
        out_specs=P("gx", "gy"),
        check_vma=False,
    )
```

```python
import jax
import jax.numpy as jnp
from jax import lax
from jax.sharding import PartitionSpec as P
from jax.experimental.layout import Layout, with_layout_constraint

CAP = 4


def body(
    tokens,
    gate_base_weight,
    up_base_weight,
    adapter_down_maps,
    adapter_up_maps,
    tenant,
    tenant_slot_index,
):
    tile_grid_rows = lax.axis_size("gx")
    tile_grid_columns = lax.axis_size("gy")
    devices = tile_grid_rows * tile_grid_columns
    row_gx = lax.axis_index("gx")
    row_gy = lax.axis_index("gy")
    local_rows = tokens.shape[0]
    tile_width = tokens.shape[1]
    total_rows = tenant.shape[0]
    block = total_rows // tile_grid_rows
    groups = local_rows // block
    tenants = tenant_slot_index.shape[0]
    column_count = gate_base_weight.shape[1]
    doubled_rank = adapter_down_maps.shape[2]
    adapter_rank_width = doubled_rank // 2
    owner_rows = tile_grid_rows * CAP

    slot_all = jnp.sum(
        jnp.where(tenant == lax.iota(jnp.int32, tenants)[None, :], tenant_slot_index[None, :], 0),
        axis=1,
    )
    onehot = (slot_all[:, None] == lax.iota(jnp.int32, devices)[None, :]).astype(jnp.int32)
    blocked = onehot.reshape(tile_grid_rows, block, devices)
    before = jnp.cumsum(blocked, axis=1) - blocked
    position = jnp.sum(before * blocked, axis=2).reshape(total_rows)

    send_slot = lax.dynamic_slice_in_dim(slot_all, row_gy * local_rows, local_rows)
    send_rank = lax.dynamic_slice_in_dim(position, row_gy * local_rows, local_rows)
    target = (send_slot * groups + lax.iota(jnp.int32, local_rows) // block) * CAP + send_rank
    outgoing = jnp.zeros((devices * groups * CAP, tile_width), jnp.bfloat16).at[target].set(tokens)
    arrived = lax.all_to_all(
        outgoing.reshape(devices, groups * CAP, tile_width),
        ("gx", "gy"),
        split_axis=0,
        concat_axis=0,
        tiled=True,
    )
    arrived = arrived.reshape(tile_grid_rows, tile_grid_columns * groups * CAP, tile_width)
    down_local = adapter_down_maps[0].reshape(tile_grid_rows, tile_width, doubled_rank)
    low = jnp.einsum("isk,ikr->sr", arrived, down_local, preferred_element_type=jnp.float32).astype(
        jnp.bfloat16
    )

    gate_up_map = adapter_up_maps[0, :adapter_rank_width].reshape(
        adapter_rank_width, tile_grid_columns, column_count
    )
    up_up_map = adapter_up_maps[0, adapter_rank_width:].reshape(
        adapter_rank_width, tile_grid_columns, column_count
    )
    delta_gate = jnp.einsum(
        "qr,rjf->jqf", low[:, :adapter_rank_width], gate_up_map, preferred_element_type=jnp.float32
    ).astype(jnp.bfloat16)
    delta_up = jnp.einsum(
        "qr,rjf->jqf", low[:, adapter_rank_width:], up_up_map, preferred_element_type=jnp.float32
    ).astype(jnp.bfloat16)
    got_gate = lax.all_to_all(delta_gate, "gy", split_axis=0, concat_axis=0, tiled=True)
    got_up = lax.all_to_all(delta_up, "gy", split_axis=0, concat_axis=0, tiled=True)
    got_gate = got_gate.reshape(tile_grid_columns * owner_rows, column_count)
    got_up = got_up.reshape(tile_grid_columns * owner_rows, column_count)

    entries = tile_grid_columns * owner_rows
    mine = slot_all // tile_grid_columns == row_gx
    entry = (slot_all % tile_grid_columns) * owner_rows + (lax.iota(jnp.int32, total_rows) // block) * CAP + position
    entry = jnp.where(mine, entry, entries)
    row_of_entry = jnp.zeros((entries,), jnp.int32).at[entry].set(
        lax.iota(jnp.int32, total_rows), mode="drop"
    )

    gathered = lax.all_gather(tokens, "gy", axis=0, tiled=True)
    row_major = Layout(major_to_minor=(0, 1))
    gate_part = with_layout_constraint(
        jnp.dot(gathered, gate_base_weight, preferred_element_type=jnp.float32).astype(jnp.bfloat16),
        row_major,
    )
    gate_part = gate_part.at[row_of_entry].add(got_gate)
    gate_sum = lax.psum_scatter(gate_part, "gx", scatter_dimension=0, tiled=True).astype(jnp.float32)
    up_part = with_layout_constraint(
        jnp.dot(gathered, up_base_weight, preferred_element_type=jnp.float32).astype(jnp.bfloat16),
        row_major,
    )
    up_part = up_part.at[row_of_entry].add(got_up)
    up_sum = lax.psum_scatter(up_part, "gx", scatter_dimension=0, tiled=True).astype(jnp.float32)
    return (jax.nn.silu(gate_sum) * up_sum).astype(jnp.bfloat16)


def solution(mesh):
    return jax.shard_map(
        body,
        mesh=mesh,
        in_specs=(
            P("gy", "gx"),
            P("gx", "gy"),
            P("gx", "gy"),
            P(("gx", "gy"), None, None),
            P(("gx", "gy"), None, None),
            P(),
            P(),
        ),
        out_specs=P("gx", "gy"),
        check_vma=False,
    )
```

```python
import jax
import jax.numpy as jnp
from jax import lax
from jax.sharding import PartitionSpec as P
from jax.experimental.layout import Layout, with_layout_constraint

CAP = 4


def body(
    tokens,
    gate_base_weight,
    up_base_weight,
    adapter_down_maps,
    adapter_up_maps,
    tenant,
    tenant_slot_index,
):
    tile_grid_rows = lax.axis_size("gx")
    tile_grid_columns = lax.axis_size("gy")
    devices = tile_grid_rows * tile_grid_columns
    row_gx = lax.axis_index("gx")
    row_gy = lax.axis_index("gy")
    local_rows = tokens.shape[0]
    tile_width = tokens.shape[1]
    total_rows = tenant.shape[0]
    block = total_rows // tile_grid_rows
    groups = local_rows // block
    tenants = tenant_slot_index.shape[0]
    column_count = gate_base_weight.shape[1]
    doubled_rank = adapter_down_maps.shape[2]
    adapter_rank_width = doubled_rank // 2
    owner_rows = tile_grid_rows * CAP

    slot_all = jnp.sum(
        jnp.where(tenant == lax.iota(jnp.int32, tenants)[None, :], tenant_slot_index[None, :], 0),
        axis=1,
    )
    onehot = (slot_all[:, None] == lax.iota(jnp.int32, devices)[None, :]).astype(jnp.int32)
    blocked = onehot.reshape(tile_grid_rows, block, devices)
    before = jnp.cumsum(blocked, axis=1) - blocked
    position = jnp.sum(before * blocked, axis=2).reshape(total_rows)

    send_slot = lax.dynamic_slice_in_dim(slot_all, row_gy * local_rows, local_rows)
    send_rank = lax.dynamic_slice_in_dim(position, row_gy * local_rows, local_rows)
    target = (send_slot * groups + lax.iota(jnp.int32, local_rows) // block) * CAP + send_rank
    outgoing = jnp.zeros((devices * groups * CAP, tile_width), jnp.bfloat16).at[target].set(tokens)
    arrived = lax.all_to_all(
        outgoing.reshape(devices, groups * CAP, tile_width),
        ("gx", "gy"),
        split_axis=0,
        concat_axis=0,
        tiled=True,
    )
    arrived = arrived.reshape(tile_grid_rows, tile_grid_columns * groups * CAP, tile_width)
    down_local = adapter_down_maps[0].reshape(tile_grid_rows, tile_width, doubled_rank)
    low = jnp.einsum("isk,ikr->sr", arrived, down_local, preferred_element_type=jnp.float32).astype(
        jnp.bfloat16
    )

    pieces = []
    for shift in range(tile_grid_columns):
        dest = (row_gy + shift) % tile_grid_columns
        piece = lax.dynamic_slice_in_dim(adapter_up_maps[0], dest * column_count, column_count, axis=1)
        if shift:
            piece = lax.ppermute(
                piece,
                "gy",
                [(src_gy, (src_gy + shift) % tile_grid_columns) for src_gy in range(tile_grid_columns)],
            )
        pieces.append(piece)
    got_maps = jnp.stack(pieces)
    low_all = lax.all_gather(low, "gy", axis=0, tiled=False)
    sources = (row_gy - lax.iota(jnp.int32, tile_grid_columns)) % tile_grid_columns
    low_all = jnp.take(low_all, sources, axis=0)
    delta_gate = jnp.einsum(
        "jqr,jrf->jqf", low_all[:, :, :adapter_rank_width], got_maps[:, :adapter_rank_width],
        preferred_element_type=jnp.float32,
    ).astype(jnp.bfloat16)
    delta_up = jnp.einsum(
        "jqr,jrf->jqf", low_all[:, :, adapter_rank_width:], got_maps[:, adapter_rank_width:],
        preferred_element_type=jnp.float32,
    ).astype(jnp.bfloat16)
    delta_gate = delta_gate.reshape(tile_grid_columns, tile_grid_rows, CAP, column_count)
    delta_up = delta_up.reshape(tile_grid_columns, tile_grid_rows, CAP, column_count)

    mine = slot_all // tile_grid_columns == row_gx
    pick = (
        mine[:, None, None]
        & (((row_gy - slot_all) % tile_grid_columns)[:, None, None] == lax.iota(jnp.int32, tile_grid_columns)[None, :, None])
        & (position[:, None, None] == lax.iota(jnp.int32, CAP)[None, None, :])
    ).astype(jnp.bfloat16).reshape(tile_grid_rows, block, tile_grid_columns, CAP)
    add_gate = jnp.einsum("bpjc,jbcf->bpf", pick, delta_gate, preferred_element_type=jnp.float32).astype(jnp.bfloat16)
    add_up = jnp.einsum("bpjc,jbcf->bpf", pick, delta_up, preferred_element_type=jnp.float32).astype(jnp.bfloat16)
    add_gate = add_gate.reshape(total_rows, column_count)
    add_up = add_up.reshape(total_rows, column_count)

    gathered = lax.all_gather(tokens, "gy", axis=0, tiled=True)
    row_major = Layout(major_to_minor=(0, 1))
    gate_part = with_layout_constraint(
        (jnp.dot(gathered, gate_base_weight, preferred_element_type=jnp.float32) + add_gate.astype(jnp.float32)).astype(jnp.bfloat16),
        row_major,
    )
    gate_sum = lax.psum_scatter(gate_part, "gx", scatter_dimension=0, tiled=True).astype(jnp.float32)
    up_part = with_layout_constraint(
        (jnp.dot(gathered, up_base_weight, preferred_element_type=jnp.float32) + add_up.astype(jnp.float32)).astype(jnp.bfloat16),
        row_major,
    )
    up_sum = lax.psum_scatter(up_part, "gx", scatter_dimension=0, tiled=True).astype(jnp.float32)
    return (jax.nn.silu(gate_sum) * up_sum).astype(jnp.bfloat16)


def solution(mesh):
    return jax.shard_map(
        body,
        mesh=mesh,
        in_specs=(
            P("gy", "gx"),
            P("gx", "gy"),
            P("gx", "gy"),
            P(("gx", "gy"), None, None),
            P(("gx", "gy"), None, None),
            P(),
            P(),
        ),
        out_specs=P("gx", "gy"),
        check_vma=False,
    )
```

```python
import jax
import jax.numpy as jnp
from jax import lax
from jax.sharding import PartitionSpec as P
from jax.experimental.layout import Layout, with_layout_constraint

CAP = 4


def body(
    tokens,
    gate_base_weight,
    up_base_weight,
    adapter_down_maps,
    adapter_up_maps,
    tenant,
    tenant_slot_index,
):
    tile_grid_rows = lax.axis_size("gx")
    tile_grid_columns = lax.axis_size("gy")
    devices = tile_grid_rows * tile_grid_columns
    row_gx = lax.axis_index("gx")
    row_gy = lax.axis_index("gy")
    local_rows = tokens.shape[0]
    tile_width = tokens.shape[1]
    total_rows = tenant.shape[0]
    block = total_rows // tile_grid_rows
    groups = local_rows // block
    tenants = tenant_slot_index.shape[0]
    column_count = gate_base_weight.shape[1]
    doubled_rank = adapter_down_maps.shape[2]
    adapter_rank_width = doubled_rank // 2
    owner_rows = tile_grid_rows * CAP

    slot_all = jnp.sum(
        jnp.where(tenant == lax.iota(jnp.int32, tenants)[None, :], tenant_slot_index[None, :], 0),
        axis=1,
    )
    onehot = (slot_all[:, None] == lax.iota(jnp.int32, devices)[None, :]).astype(jnp.int32)
    blocked = onehot.reshape(tile_grid_rows, block, devices)
    before = jnp.cumsum(blocked, axis=1) - blocked
    position = jnp.sum(before * blocked, axis=2).reshape(total_rows)

    send_slot = lax.dynamic_slice_in_dim(slot_all, row_gy * local_rows, local_rows)
    send_rank = lax.dynamic_slice_in_dim(position, row_gy * local_rows, local_rows)
    target = (send_slot * groups + lax.iota(jnp.int32, local_rows) // block) * CAP + send_rank
    outgoing = jnp.zeros((devices * groups * CAP, tile_width), jnp.bfloat16).at[target].set(tokens)
    arrived = lax.all_to_all(
        outgoing.reshape(devices, groups * CAP, tile_width),
        ("gx", "gy"),
        split_axis=0,
        concat_axis=0,
        tiled=True,
    )
    arrived = arrived.reshape(tile_grid_rows, tile_grid_columns * groups * CAP, tile_width)
    down_local = adapter_down_maps[0].reshape(tile_grid_rows, tile_width, doubled_rank)
    low = jnp.einsum("isk,ikr->sr", arrived, down_local, preferred_element_type=jnp.float32).astype(
        jnp.bfloat16
    )

    gate_up_map = adapter_up_maps[0, :adapter_rank_width].reshape(
        adapter_rank_width, tile_grid_columns, column_count
    )
    up_up_map = adapter_up_maps[0, adapter_rank_width:].reshape(
        adapter_rank_width, tile_grid_columns, column_count
    )
    delta_gate = jnp.einsum(
        "qr,rjf->jqf", low[:, :adapter_rank_width], gate_up_map, preferred_element_type=jnp.float32
    ).astype(jnp.bfloat16)
    delta_up = jnp.einsum(
        "qr,rjf->jqf", low[:, adapter_rank_width:], up_up_map, preferred_element_type=jnp.float32
    ).astype(jnp.bfloat16)
    got_gate = lax.all_to_all(delta_gate, "gy", split_axis=0, concat_axis=0, tiled=True)
    got_up = lax.all_to_all(delta_up, "gy", split_axis=0, concat_axis=0, tiled=True)

    got_gate = got_gate.reshape(tile_grid_columns, tile_grid_rows, CAP, column_count)
    got_up = got_up.reshape(tile_grid_columns, tile_grid_rows, CAP, column_count)
    mine = slot_all // tile_grid_columns == row_gx
    pick = (
        mine[:, None, None]
        & ((slot_all % tile_grid_columns)[:, None, None] == lax.iota(jnp.int32, tile_grid_columns)[None, :, None])
        & (position[:, None, None] == lax.iota(jnp.int32, CAP)[None, None, :])
    ).astype(jnp.bfloat16).reshape(tile_grid_rows, block, tile_grid_columns, CAP)

    gathered = lax.all_gather(tokens, "gy", axis=0, tiled=True)
    row_major = Layout(major_to_minor=(0, 1))
    gate_part = with_layout_constraint(
        jnp.dot(gathered, gate_base_weight, preferred_element_type=jnp.float32).astype(jnp.bfloat16),
        row_major,
    )
    gate_part = (
        jnp.einsum("bpjc,jbcf->bpf", pick, got_gate, preferred_element_type=jnp.float32).reshape(total_rows, column_count)
        + lax.optimization_barrier(gate_part).astype(jnp.float32)
    ).astype(jnp.bfloat16)
    gate_sum = lax.psum_scatter(gate_part, "gx", scatter_dimension=0, tiled=True).astype(jnp.float32)
    up_part = with_layout_constraint(
        jnp.dot(gathered, up_base_weight, preferred_element_type=jnp.float32).astype(jnp.bfloat16),
        row_major,
    )
    up_part = (
        jnp.einsum("bpjc,jbcf->bpf", pick, got_up, preferred_element_type=jnp.float32).reshape(total_rows, column_count)
        + lax.optimization_barrier(up_part).astype(jnp.float32)
    ).astype(jnp.bfloat16)
    up_sum = lax.psum_scatter(up_part, "gx", scatter_dimension=0, tiled=True).astype(jnp.float32)
    return (jax.nn.silu(gate_sum) * up_sum).astype(jnp.bfloat16)


def solution(mesh):
    return jax.shard_map(
        body,
        mesh=mesh,
        in_specs=(
            P("gy", "gx"),
            P("gx", "gy"),
            P("gx", "gy"),
            P(("gx", "gy"), None, None),
            P(("gx", "gy"), None, None),
            P(),
            P(),
        ),
        out_specs=P("gx", "gy"),
        check_vma=False,
    )
```

```python
import jax
import jax.numpy as jnp
from jax import lax
from jax.sharding import PartitionSpec as P
from jax.experimental.layout import Layout, with_layout_constraint

CAP = 4


def body(
    tokens,
    gate_base_weight,
    up_base_weight,
    adapter_down_maps,
    adapter_up_maps,
    tenant,
    tenant_slot_index,
):
    tile_grid_rows = lax.axis_size("gx")
    tile_grid_columns = lax.axis_size("gy")
    devices = tile_grid_rows * tile_grid_columns
    row_gx = lax.axis_index("gx")
    row_gy = lax.axis_index("gy")
    local_rows = tokens.shape[0]
    tile_width = tokens.shape[1]
    total_rows = tenant.shape[0]
    block = total_rows // tile_grid_rows
    groups = local_rows // block
    tenants = tenant_slot_index.shape[0]
    column_count = gate_base_weight.shape[1]
    doubled_rank = adapter_down_maps.shape[2]
    adapter_rank_width = doubled_rank // 2
    owner_rows = tile_grid_rows * CAP

    slot_all = jnp.sum(
        jnp.where(tenant == lax.iota(jnp.int32, tenants)[None, :], tenant_slot_index[None, :], 0),
        axis=1,
    )
    onehot = (slot_all[:, None] == lax.iota(jnp.int32, devices)[None, :]).astype(jnp.int32)
    blocked = onehot.reshape(tile_grid_rows, block, devices)
    before = jnp.cumsum(blocked, axis=1) - blocked
    position = jnp.sum(before * blocked, axis=2).reshape(total_rows)

    send_slot = lax.dynamic_slice_in_dim(slot_all, row_gy * local_rows, local_rows)
    send_rank = lax.dynamic_slice_in_dim(position, row_gy * local_rows, local_rows)
    target = (send_slot * groups + lax.iota(jnp.int32, local_rows) // block) * CAP + send_rank
    outgoing = jnp.zeros((devices * groups * CAP, tile_width), jnp.bfloat16).at[target].set(tokens)
    arrived = lax.all_to_all(
        outgoing.reshape(devices, groups * CAP, tile_width),
        ("gx", "gy"),
        split_axis=0,
        concat_axis=0,
        tiled=True,
    )
    arrived = arrived.reshape(tile_grid_rows, tile_grid_columns * groups * CAP, tile_width)
    down_local = adapter_down_maps[0].reshape(tile_grid_rows, tile_width, doubled_rank)
    low = jnp.einsum("isk,ikr->sr", arrived, down_local, preferred_element_type=jnp.float32).astype(
        jnp.bfloat16
    )

    gate_up_map = adapter_up_maps[0, :adapter_rank_width].reshape(
        adapter_rank_width, tile_grid_columns, column_count
    )
    up_up_map = adapter_up_maps[0, adapter_rank_width:].reshape(
        adapter_rank_width, tile_grid_columns, column_count
    )
    split = (column_count // 2) // 128 * 128
    bounds = [(0, split), (split, column_count)]
    got_gate = []
    for lo, hi in bounds:
        piece = jnp.einsum(
            "qr,rjf->jqf", low[:, :adapter_rank_width], gate_up_map[:, :, lo:hi], preferred_element_type=jnp.float32
        ).astype(jnp.bfloat16)
        piece = lax.all_to_all(piece, "gy", split_axis=0, concat_axis=0, tiled=True)
        got_gate.append(piece.reshape(tile_grid_columns * owner_rows, hi - lo))
    delta_up = jnp.einsum(
        "qr,rjf->jqf", low[:, adapter_rank_width:], up_up_map, preferred_element_type=jnp.float32
    ).astype(jnp.bfloat16)
    got_up = lax.all_to_all(delta_up, "gy", split_axis=0, concat_axis=0, tiled=True)
    got_up = got_up.reshape(tile_grid_columns * owner_rows, column_count)

    entries = tile_grid_columns * owner_rows
    mine = slot_all // tile_grid_columns == row_gx
    entry = (slot_all % tile_grid_columns) * owner_rows + (lax.iota(jnp.int32, total_rows) // block) * CAP + position
    entry = jnp.where(mine, entry, entries)
    row_of_entry = jnp.zeros((entries,), jnp.int32).at[entry].set(
        lax.iota(jnp.int32, total_rows), mode="drop"
    )

    gathered = lax.all_gather(tokens, "gy", axis=0, tiled=True)
    row_major = Layout(major_to_minor=(0, 1))
    gate_sums = []
    for (lo, hi), got in zip(bounds, got_gate):
        part = with_layout_constraint(
            jnp.dot(gathered, gate_base_weight[:, lo:hi], preferred_element_type=jnp.float32).astype(jnp.bfloat16),
            row_major,
        )
        part = part.at[row_of_entry].add(got)
        gate_sums.append(lax.psum_scatter(part, "gx", scatter_dimension=0, tiled=True))
    gate_sum = jnp.concatenate(gate_sums, axis=1).astype(jnp.float32)
    up_part = with_layout_constraint(
        jnp.dot(gathered, up_base_weight, preferred_element_type=jnp.float32).astype(jnp.bfloat16),
        row_major,
    )
    up_part = up_part.at[row_of_entry].add(got_up)
    up_sum = lax.psum_scatter(up_part, "gx", scatter_dimension=0, tiled=True).astype(jnp.float32)
    return (jax.nn.silu(gate_sum) * up_sum).astype(jnp.bfloat16)


def solution(mesh):
    return jax.shard_map(
        body,
        mesh=mesh,
        in_specs=(
            P("gy", "gx"),
            P("gx", "gy"),
            P("gx", "gy"),
            P(("gx", "gy"), None, None),
            P(("gx", "gy"), None, None),
            P(),
            P(),
        ),
        out_specs=P("gx", "gy"),
        check_vma=False,
    )
```

```python
import jax
import jax.numpy as jnp
from jax import lax
from jax.sharding import PartitionSpec as P
from jax.experimental.layout import Layout, with_layout_constraint

CAP = 4


def body(
    tokens,
    gate_base_weight,
    up_base_weight,
    adapter_down_maps,
    adapter_up_maps,
    tenant,
    tenant_slot_index,
):
    tile_grid_rows = lax.axis_size("gx")
    tile_grid_columns = lax.axis_size("gy")
    devices = tile_grid_rows * tile_grid_columns
    row_gx = lax.axis_index("gx")
    row_gy = lax.axis_index("gy")
    local_rows = tokens.shape[0]
    tile_width = tokens.shape[1]
    total_rows = tenant.shape[0]
    block = total_rows // tile_grid_rows
    groups = local_rows // block
    tenants = tenant_slot_index.shape[0]
    column_count = gate_base_weight.shape[1]
    doubled_rank = adapter_down_maps.shape[2]
    adapter_rank_width = doubled_rank // 2
    owner_rows = tile_grid_rows * CAP

    slot_all = jnp.sum(
        jnp.where(tenant == lax.iota(jnp.int32, tenants)[None, :], tenant_slot_index[None, :], 0),
        axis=1,
    )
    onehot = (slot_all[:, None] == lax.iota(jnp.int32, devices)[None, :]).astype(jnp.int32)
    blocked = onehot.reshape(tile_grid_rows, block, devices)
    before = jnp.cumsum(blocked, axis=1) - blocked
    position = jnp.sum(before * blocked, axis=2).reshape(total_rows)

    send_slot = lax.dynamic_slice_in_dim(slot_all, row_gy * local_rows, local_rows)
    send_rank = lax.dynamic_slice_in_dim(position, row_gy * local_rows, local_rows)
    target = (send_slot * groups + lax.iota(jnp.int32, local_rows) // block) * CAP + send_rank
    outgoing = jnp.zeros((devices * groups * CAP, tile_width), jnp.bfloat16).at[target].set(tokens)
    arrived = lax.all_to_all(
        outgoing.reshape(devices, groups * CAP, tile_width),
        ("gx", "gy"),
        split_axis=0,
        concat_axis=0,
        tiled=True,
    )
    arrived = arrived.reshape(tile_grid_rows, tile_grid_columns * groups * CAP, tile_width)
    down_local = adapter_down_maps[0].reshape(tile_grid_rows, tile_width, doubled_rank)
    low = jnp.einsum("isk,ikr->sr", arrived, down_local, preferred_element_type=jnp.float32).astype(
        jnp.bfloat16
    )

    gate_up_map = adapter_up_maps[0, :adapter_rank_width].reshape(
        adapter_rank_width, tile_grid_columns, column_count
    )
    up_up_map = adapter_up_maps[0, adapter_rank_width:].reshape(
        adapter_rank_width, tile_grid_columns, column_count
    )
    delta_gate = jnp.einsum(
        "qr,rjf->jqf", low[:, :adapter_rank_width], gate_up_map, preferred_element_type=jnp.float32
    ).astype(jnp.bfloat16)
    delta_up = jnp.einsum(
        "qr,rjf->jqf", low[:, adapter_rank_width:], up_up_map, preferred_element_type=jnp.float32
    ).astype(jnp.bfloat16)
    got_gate = lax.all_to_all(delta_gate, "gy", split_axis=0, concat_axis=0, tiled=True)
    got_up = lax.all_to_all(delta_up, "gy", split_axis=0, concat_axis=0, tiled=True)
    got_gate = got_gate.reshape(tile_grid_columns * owner_rows, column_count)
    got_up = got_up.reshape(tile_grid_columns * owner_rows, column_count)

    entries = tile_grid_columns * owner_rows
    mine = slot_all // tile_grid_columns == row_gx
    entry = (slot_all % tile_grid_columns) * owner_rows + (lax.iota(jnp.int32, total_rows) // block) * CAP + position
    entry = jnp.where(mine, entry, entries)
    spare_rank = jnp.cumsum(jnp.where(mine, 0, 1)) - 1
    spare_rows = jnp.zeros((entries,), jnp.int32).at[jnp.where(mine, entries, spare_rank)].set(
        lax.iota(jnp.int32, total_rows), mode="drop"
    )
    row_of_entry = spare_rows.at[entry].set(lax.iota(jnp.int32, total_rows), mode="drop")

    gathered = lax.all_gather(tokens, "gy", axis=0, tiled=True)
    row_major = Layout(major_to_minor=(0, 1))
    gate_part = with_layout_constraint(
        jnp.dot(gathered, gate_base_weight, preferred_element_type=jnp.float32).astype(jnp.bfloat16),
        row_major,
    )
    gate_part = gate_part.at[row_of_entry].add(got_gate, unique_indices=True, mode="promise_in_bounds")
    gate_sum = lax.psum_scatter(gate_part, "gx", scatter_dimension=0, tiled=True).astype(jnp.float32)
    up_part = with_layout_constraint(
        jnp.dot(gathered, up_base_weight, preferred_element_type=jnp.float32).astype(jnp.bfloat16),
        row_major,
    )
    up_part = up_part.at[row_of_entry].add(got_up, unique_indices=True, mode="promise_in_bounds")
    up_sum = lax.psum_scatter(up_part, "gx", scatter_dimension=0, tiled=True).astype(jnp.float32)
    return (jax.nn.silu(gate_sum) * up_sum).astype(jnp.bfloat16)


def solution(mesh):
    return jax.shard_map(
        body,
        mesh=mesh,
        in_specs=(
            P("gy", "gx"),
            P("gx", "gy"),
            P("gx", "gy"),
            P(("gx", "gy"), None, None),
            P(("gx", "gy"), None, None),
            P(),
            P(),
        ),
        out_specs=P("gx", "gy"),
        check_vma=False,
    )
```

```python
import jax
import jax.numpy as jnp
from jax import lax
from jax.sharding import PartitionSpec as P
from jax.experimental.layout import Layout, with_layout_constraint

CAP = 4


def body(
    tokens,
    gate_base_weight,
    up_base_weight,
    adapter_down_maps,
    adapter_up_maps,
    tenant,
    tenant_slot_index,
):
    tile_grid_rows = lax.axis_size("gx")
    tile_grid_columns = lax.axis_size("gy")
    devices = tile_grid_rows * tile_grid_columns
    row_gx = lax.axis_index("gx")
    row_gy = lax.axis_index("gy")
    local_rows = tokens.shape[0]
    tile_width = tokens.shape[1]
    total_rows = tenant.shape[0]
    block = total_rows // tile_grid_rows
    groups = local_rows // block
    tenants = tenant_slot_index.shape[0]
    column_count = gate_base_weight.shape[1]
    doubled_rank = adapter_down_maps.shape[2]
    adapter_rank_width = doubled_rank // 2
    gathered = lax.all_gather(tokens, "gy", axis=0, tiled=True)
    both_weights = jnp.concatenate([gate_base_weight, up_base_weight], axis=1)
    partial = with_layout_constraint(
        jnp.dot(gathered, both_weights, preferred_element_type=jnp.float32).astype(jnp.bfloat16),
        Layout(major_to_minor=(0, 1)),
    )
    summed = lax.psum_scatter(partial, "gx", scatter_dimension=0, tiled=True)
    slot_all = jnp.sum(
        jnp.where(tenant == lax.iota(jnp.int32, tenants)[None, :], tenant_slot_index[None, :], 0),
        axis=1,
    )
    onehot = (slot_all[:, None] == lax.iota(jnp.int32, devices)[None, :]).astype(jnp.int32)
    blocked = onehot.reshape(tile_grid_rows, block, devices)
    before = jnp.cumsum(blocked, axis=1) - blocked
    position = jnp.sum(before * blocked, axis=2).reshape(total_rows)
    send_slot = lax.dynamic_slice_in_dim(slot_all, row_gy * local_rows, local_rows)
    send_rank = lax.dynamic_slice_in_dim(position, row_gy * local_rows, local_rows)
    target = (send_slot * groups + lax.iota(jnp.int32, local_rows) // block) * CAP + send_rank
    outgoing = jnp.zeros((devices * groups * CAP, tile_width), jnp.bfloat16).at[target].set(tokens)
    arrived = lax.all_to_all(
        outgoing.reshape(devices, groups * CAP, tile_width),
        ("gx", "gy"),
        split_axis=0,
        concat_axis=0,
        tiled=True,
    )
    arrived = arrived.reshape(tile_grid_rows, tile_grid_columns * groups * CAP, tile_width)
    down_local = adapter_down_maps[0].reshape(tile_grid_rows, tile_width, doubled_rank)
    low = jnp.einsum("isk,ikr->sr", arrived, down_local, preferred_element_type=jnp.float32).astype(
        jnp.bfloat16
    )
    low = low.reshape(tile_grid_rows, CAP, doubled_rank)
    gate_up_map = adapter_up_maps[0, :adapter_rank_width].reshape(
        adapter_rank_width, tile_grid_columns, column_count
    )
    up_up_map = adapter_up_maps[0, adapter_rank_width:].reshape(
        adapter_rank_width, tile_grid_columns, column_count
    )
    delta_gate = jnp.einsum(
        "gcr,rjf->gjcf",
        low[:, :, :adapter_rank_width],
        gate_up_map,
        preferred_element_type=jnp.float32,
    ).astype(jnp.bfloat16)
    delta_up = jnp.einsum(
        "gcr,rjf->gjcf",
        low[:, :, adapter_rank_width:],
        up_up_map,
        preferred_element_type=jnp.float32,
    ).astype(jnp.bfloat16)
    delta = jnp.concatenate(
        [delta_gate.reshape(devices, CAP, column_count), delta_up.reshape(devices, CAP, column_count)], axis=2
    )
    summed, delta = lax.optimization_barrier((summed, delta))
    back = lax.all_to_all(delta, ("gx", "gy"), split_axis=0, concat_axis=0, tiled=True)
    back = back.reshape(devices * CAP, 2 * column_count)
    own_slot = lax.dynamic_slice_in_dim(slot_all, row_gx * block, block)
    own_rank = lax.dynamic_slice_in_dim(position, row_gx * block, block)
    pick = own_slot * CAP + own_rank
    picked = back[pick].astype(jnp.float32)
    summed = summed.astype(jnp.float32)
    gate_value = summed[:, :column_count] + picked[:, :column_count]
    up_value = summed[:, column_count:] + picked[:, column_count:]
    return (jax.nn.silu(gate_value) * up_value).astype(jnp.bfloat16)


def solution(mesh):
    return jax.shard_map(
        body,
        mesh=mesh,
        in_specs=(
            P("gy", "gx"),
            P("gx", "gy"),
            P("gx", "gy"),
            P(("gx", "gy"), None, None),
            P(("gx", "gy"), None, None),
            P(),
            P(),
        ),
        out_specs=P("gx", "gy"),
        check_vma=False,
    )
```

```python
import jax
import jax.numpy as jnp
from jax import lax
from jax.sharding import PartitionSpec as P
from jax.experimental.layout import Layout, with_layout_constraint

CAP = 4


def ring_sum(chunks, ring_size, place, step_up, step_down):
    half = chunks.shape[1] // 2
    ahead, behind = chunks[:, :half], chunks[:, half:]
    send_up = lax.dynamic_index_in_dim(ahead, (place - 1) % ring_size, 0, keepdims=False)
    send_down = lax.dynamic_index_in_dim(behind, (place + 1) % ring_size, 0, keepdims=False)
    for step in range(ring_size - 1):
        got_up = lax.ppermute(send_up, "gx", step_up)
        got_down = lax.ppermute(send_down, "gx", step_down)
        sum_up = got_up.astype(jnp.float32) + lax.dynamic_index_in_dim(
            ahead, (place - 2 - step) % ring_size, 0, keepdims=False
        ).astype(jnp.float32)
        sum_down = got_down.astype(jnp.float32) + lax.dynamic_index_in_dim(
            behind, (place + 2 + step) % ring_size, 0, keepdims=False
        ).astype(jnp.float32)
        send_up, send_down = sum_up.astype(jnp.bfloat16), sum_down.astype(jnp.bfloat16)
    return jnp.concatenate([sum_up, sum_down], axis=0)


def torus_reduce_scatter(part, outer, inner):
    here = lax.axis_index("gx")
    here_outer, here_inner = here // inner, here % inner
    rows = part.shape[0] // (outer * inner)
    blocks = part.reshape(outer, inner, rows, part.shape[1])

    def shift(o, i):
        return [(a * inner + b, ((a + o) % outer) * inner + (b + i) % inner) for a in range(outer) for b in range(inner)]

    by_outer = ring_sum(blocks, outer, here_outer, shift(1, 0), shift(-1, 0))
    by_inner = ring_sum(by_outer.astype(jnp.bfloat16), inner, here_inner, shift(0, 1), shift(0, -1))
    return by_inner


def body(
    tokens,
    gate_base_weight,
    up_base_weight,
    adapter_down_maps,
    adapter_up_maps,
    tenant,
    tenant_slot_index,
):
    tile_grid_rows = lax.axis_size("gx")
    tile_grid_columns = lax.axis_size("gy")
    devices = tile_grid_rows * tile_grid_columns
    row_gx = lax.axis_index("gx")
    row_gy = lax.axis_index("gy")
    local_rows = tokens.shape[0]
    tile_width = tokens.shape[1]
    total_rows = tenant.shape[0]
    block = total_rows // tile_grid_rows
    groups = local_rows // block
    tenants = tenant_slot_index.shape[0]
    column_count = gate_base_weight.shape[1]
    doubled_rank = adapter_down_maps.shape[2]
    adapter_rank_width = doubled_rank // 2
    owner_rows = tile_grid_rows * CAP

    slot_all = jnp.sum(
        jnp.where(tenant == lax.iota(jnp.int32, tenants)[None, :], tenant_slot_index[None, :], 0),
        axis=1,
    )
    onehot = (slot_all[:, None] == lax.iota(jnp.int32, devices)[None, :]).astype(jnp.int32)
    blocked = onehot.reshape(tile_grid_rows, block, devices)
    before = jnp.cumsum(blocked, axis=1) - blocked
    position = jnp.sum(before * blocked, axis=2).reshape(total_rows)

    send_slot = lax.dynamic_slice_in_dim(slot_all, row_gy * local_rows, local_rows)
    send_rank = lax.dynamic_slice_in_dim(position, row_gy * local_rows, local_rows)
    target = (send_slot * groups + lax.iota(jnp.int32, local_rows) // block) * CAP + send_rank
    outgoing = jnp.zeros((devices * groups * CAP, tile_width), jnp.bfloat16).at[target].set(tokens)
    arrived = lax.all_to_all(
        outgoing.reshape(devices, groups * CAP, tile_width),
        ("gx", "gy"),
        split_axis=0,
        concat_axis=0,
        tiled=True,
    )
    arrived = arrived.reshape(tile_grid_rows, tile_grid_columns * groups * CAP, tile_width)
    down_local = adapter_down_maps[0].reshape(tile_grid_rows, tile_width, doubled_rank)
    low = jnp.einsum("isk,ikr->sr", arrived, down_local, preferred_element_type=jnp.float32).astype(
        jnp.bfloat16
    )

    gate_up_map = adapter_up_maps[0, :adapter_rank_width].reshape(
        adapter_rank_width, tile_grid_columns, column_count
    )
    up_up_map = adapter_up_maps[0, adapter_rank_width:].reshape(
        adapter_rank_width, tile_grid_columns, column_count
    )
    delta_gate = jnp.einsum(
        "qr,rjf->jqf", low[:, :adapter_rank_width], gate_up_map, preferred_element_type=jnp.float32
    ).astype(jnp.bfloat16)
    delta_up = jnp.einsum(
        "qr,rjf->jqf", low[:, adapter_rank_width:], up_up_map, preferred_element_type=jnp.float32
    ).astype(jnp.bfloat16)
    got_gate = lax.all_to_all(delta_gate, "gy", split_axis=0, concat_axis=0, tiled=True)
    got_up = lax.all_to_all(delta_up, "gy", split_axis=0, concat_axis=0, tiled=True)
    got_gate = got_gate.reshape(tile_grid_columns * owner_rows, column_count)
    got_up = got_up.reshape(tile_grid_columns * owner_rows, column_count)

    entries = tile_grid_columns * owner_rows
    mine = slot_all // tile_grid_columns == row_gx
    entry = (slot_all % tile_grid_columns) * owner_rows + (lax.iota(jnp.int32, total_rows) // block) * CAP + position
    entry = jnp.where(mine, entry, entries)
    row_of_entry = jnp.zeros((entries,), jnp.int32).at[entry].set(
        lax.iota(jnp.int32, total_rows), mode="drop"
    )

    gathered = lax.all_gather(tokens, "gy", axis=0, tiled=True)
    row_major = Layout(major_to_minor=(0, 1))
    gate_part = with_layout_constraint(
        jnp.dot(gathered, gate_base_weight, preferred_element_type=jnp.float32).astype(jnp.bfloat16),
        row_major,
    )
    gate_part = gate_part.at[row_of_entry].add(got_gate)
    gate_sum = lax.psum_scatter(gate_part, "gx", scatter_dimension=0, tiled=True).astype(jnp.float32)
    up_part = with_layout_constraint(
        jnp.dot(gathered, up_base_weight, preferred_element_type=jnp.float32).astype(jnp.bfloat16),
        row_major,
    )
    up_part = up_part.at[row_of_entry].add(got_up)
    inner = 4 if tile_grid_rows % 4 == 0 and tile_grid_rows > 4 else 1
    if inner > 1:
        up_sum = torus_reduce_scatter(up_part, tile_grid_rows // inner, inner)
    else:
        up_sum = lax.psum_scatter(up_part, "gx", scatter_dimension=0, tiled=True).astype(jnp.float32)
    return (jax.nn.silu(gate_sum) * up_sum).astype(jnp.bfloat16)


def solution(mesh):
    return jax.shard_map(
        body,
        mesh=mesh,
        in_specs=(
            P("gy", "gx"),
            P("gx", "gy"),
            P("gx", "gy"),
            P(("gx", "gy"), None, None),
            P(("gx", "gy"), None, None),
            P(),
            P(),
        ),
        out_specs=P("gx", "gy"),
        check_vma=False,
    )
```

```python
import jax
import jax.numpy as jnp
from jax import lax
from jax.sharding import PartitionSpec as P
from jax.experimental.layout import Layout, with_layout_constraint
from jax.experimental import pallas as pl
from jax.experimental.pallas import tpu as pltpu

CAP = 4


def add_picked(pick_ref, got_ref, part_ref, out_ref):
    added = jnp.dot(pick_ref[0], got_ref[0], preferred_element_type=jnp.float32)
    out_ref[0] = (part_ref[0].astype(jnp.float32) + added).astype(out_ref.dtype)


def body(
    tokens,
    gate_base_weight,
    up_base_weight,
    adapter_down_maps,
    adapter_up_maps,
    tenant,
    tenant_slot_index,
):
    tile_grid_rows = lax.axis_size("gx")
    tile_grid_columns = lax.axis_size("gy")
    devices = tile_grid_rows * tile_grid_columns
    row_gx = lax.axis_index("gx")
    row_gy = lax.axis_index("gy")
    local_rows = tokens.shape[0]
    tile_width = tokens.shape[1]
    total_rows = tenant.shape[0]
    block = total_rows // tile_grid_rows
    groups = local_rows // block
    tenants = tenant_slot_index.shape[0]
    column_count = gate_base_weight.shape[1]
    doubled_rank = adapter_down_maps.shape[2]
    adapter_rank_width = doubled_rank // 2
    owner_rows = tile_grid_rows * CAP

    slot_all = jnp.sum(
        jnp.where(tenant == lax.iota(jnp.int32, tenants)[None, :], tenant_slot_index[None, :], 0),
        axis=1,
    )
    onehot = (slot_all[:, None] == lax.iota(jnp.int32, devices)[None, :]).astype(jnp.int32)
    blocked = onehot.reshape(tile_grid_rows, block, devices)
    before = jnp.cumsum(blocked, axis=1) - blocked
    position = jnp.sum(before * blocked, axis=2).reshape(total_rows)

    send_slot = lax.dynamic_slice_in_dim(slot_all, row_gy * local_rows, local_rows)
    send_rank = lax.dynamic_slice_in_dim(position, row_gy * local_rows, local_rows)
    target = (send_slot * groups + lax.iota(jnp.int32, local_rows) // block) * CAP + send_rank
    outgoing = jnp.zeros((devices * groups * CAP, tile_width), jnp.bfloat16).at[target].set(tokens)
    arrived = lax.all_to_all(
        outgoing.reshape(devices, groups * CAP, tile_width),
        ("gx", "gy"),
        split_axis=0,
        concat_axis=0,
        tiled=True,
    )
    arrived = arrived.reshape(tile_grid_rows, tile_grid_columns * groups * CAP, tile_width)
    down_local = adapter_down_maps[0].reshape(tile_grid_rows, tile_width, doubled_rank)
    low = jnp.einsum("isk,ikr->sr", arrived, down_local, preferred_element_type=jnp.float32).astype(
        jnp.bfloat16
    )

    gate_up_map = adapter_up_maps[0, :adapter_rank_width].reshape(
        adapter_rank_width, tile_grid_columns, column_count
    )
    up_up_map = adapter_up_maps[0, adapter_rank_width:].reshape(
        adapter_rank_width, tile_grid_columns, column_count
    )
    delta_gate = jnp.einsum(
        "qr,rjf->jqf", low[:, :adapter_rank_width], gate_up_map, preferred_element_type=jnp.float32
    ).astype(jnp.bfloat16)
    delta_up = jnp.einsum(
        "qr,rjf->jqf", low[:, adapter_rank_width:], up_up_map, preferred_element_type=jnp.float32
    ).astype(jnp.bfloat16)
    got_gate = lax.all_to_all(delta_gate, "gy", split_axis=0, concat_axis=0, tiled=True)
    got_up = lax.all_to_all(delta_up, "gy", split_axis=0, concat_axis=0, tiled=True)

    got_gate = jnp.swapaxes(got_gate.reshape(tile_grid_columns, tile_grid_rows, CAP, column_count), 0, 1)
    got_gate = got_gate.reshape(tile_grid_rows, tile_grid_columns * CAP, column_count)
    got_up = jnp.swapaxes(got_up.reshape(tile_grid_columns, tile_grid_rows, CAP, column_count), 0, 1)
    got_up = got_up.reshape(tile_grid_rows, tile_grid_columns * CAP, column_count)
    mine = slot_all // tile_grid_columns == row_gx
    lane = (slot_all % tile_grid_columns) * CAP + position
    pick = (mine[:, None] & (lane[:, None] == lax.iota(jnp.int32, tile_grid_columns * CAP)[None, :]))
    pick = pick.astype(jnp.bfloat16).reshape(tile_grid_rows, block, tile_grid_columns * CAP)

    def with_delta(part, got):
        blocks = part.reshape(tile_grid_rows, block, column_count)
        lanes = got.shape[1]
        out = pl.pallas_call(
            add_picked,
            out_shape=jax.ShapeDtypeStruct(blocks.shape, blocks.dtype),
            grid=(tile_grid_rows,),
            in_specs=[
                pl.BlockSpec((1, block, lanes), lambda b: (b, 0, 0)),
                pl.BlockSpec((1, lanes, column_count), lambda b: (b, 0, 0)),
                pl.BlockSpec((1, block, column_count), lambda b: (b, 0, 0)),
            ],
            out_specs=pl.BlockSpec((1, block, column_count), lambda b: (b, 0, 0)),
            input_output_aliases={2: 0},
            cost_estimate=pl.CostEstimate(
                flops=2 * tile_grid_rows * block * lanes * column_count,
                transcendentals=0,
                bytes_accessed=2 * (2 * blocks.size + got.size + pick.size),
            ),
        )(pick, got, blocks)
        return out.reshape(total_rows, column_count)

    gathered = lax.all_gather(tokens, "gy", axis=0, tiled=True)
    row_major = Layout(major_to_minor=(0, 1))
    gate_part = with_layout_constraint(
        jnp.dot(gathered, gate_base_weight, preferred_element_type=jnp.float32).astype(jnp.bfloat16),
        row_major,
    )
    gate_part = with_delta(gate_part, got_gate)
    gate_sum = lax.psum_scatter(gate_part, "gx", scatter_dimension=0, tiled=True).astype(jnp.float32)
    up_part = with_layout_constraint(
        jnp.dot(gathered, up_base_weight, preferred_element_type=jnp.float32).astype(jnp.bfloat16),
        row_major,
    )
    up_part = with_delta(up_part, got_up)
    up_sum = lax.psum_scatter(up_part, "gx", scatter_dimension=0, tiled=True).astype(jnp.float32)
    return (jax.nn.silu(gate_sum) * up_sum).astype(jnp.bfloat16)


def solution(mesh):
    return jax.shard_map(
        body,
        mesh=mesh,
        in_specs=(
            P("gy", "gx"),
            P("gx", "gy"),
            P("gx", "gy"),
            P(("gx", "gy"), None, None),
            P(("gx", "gy"), None, None),
            P(),
            P(),
        ),
        out_specs=P("gx", "gy"),
        check_vma=False,
    )
```

```python
import jax
import jax.numpy as jnp
from jax import lax
from jax.sharding import PartitionSpec as P
from jax.experimental.layout import Layout, with_layout_constraint

CAP = 4


def body(
    tokens,
    gate_base_weight,
    up_base_weight,
    adapter_down_maps,
    adapter_up_maps,
    tenant,
    tenant_slot_index,
):
    tile_grid_rows = lax.axis_size("gx")
    tile_grid_columns = lax.axis_size("gy")
    devices = tile_grid_rows * tile_grid_columns
    row_gx = lax.axis_index("gx")
    row_gy = lax.axis_index("gy")
    local_rows = tokens.shape[0]
    tile_width = tokens.shape[1]
    total_rows = tenant.shape[0]
    block = total_rows // tile_grid_rows
    groups = local_rows // block
    tenants = tenant_slot_index.shape[0]
    column_count = gate_base_weight.shape[1]
    doubled_rank = adapter_down_maps.shape[2]
    adapter_rank_width = doubled_rank // 2
    owner_rows = tile_grid_rows * CAP

    slot_all = jnp.sum(
        jnp.where(tenant == lax.iota(jnp.int32, tenants)[None, :], tenant_slot_index[None, :], 0),
        axis=1,
    )
    onehot = (slot_all[:, None] == lax.iota(jnp.int32, devices)[None, :]).astype(jnp.int32)
    blocked = onehot.reshape(tile_grid_rows, block, devices)
    before = jnp.cumsum(blocked, axis=1) - blocked
    position = jnp.sum(before * blocked, axis=2).reshape(total_rows)

    send_slot = lax.dynamic_slice_in_dim(slot_all, row_gy * local_rows, local_rows)
    send_rank = lax.dynamic_slice_in_dim(position, row_gy * local_rows, local_rows)
    target = (send_slot * groups + lax.iota(jnp.int32, local_rows) // block) * CAP + send_rank
    outgoing = jnp.zeros((devices * groups * CAP, tile_width), jnp.bfloat16).at[target].set(tokens)
    arrived = lax.all_to_all(
        outgoing.reshape(devices, groups * CAP, tile_width),
        ("gx", "gy"),
        split_axis=0,
        concat_axis=0,
        tiled=True,
    )
    arrived = arrived.reshape(tile_grid_rows, tile_grid_columns * groups * CAP, tile_width)
    down_local = adapter_down_maps[0].reshape(tile_grid_rows, tile_width, doubled_rank)
    low = jnp.einsum("isk,ikr->sr", arrived, down_local, preferred_element_type=jnp.float32).astype(
        jnp.bfloat16
    )

    gate_up_map = adapter_up_maps[0, :adapter_rank_width].reshape(
        adapter_rank_width, tile_grid_columns, column_count
    )
    up_up_map = adapter_up_maps[0, adapter_rank_width:].reshape(
        adapter_rank_width, tile_grid_columns, column_count
    )
    delta_gate = jnp.einsum(
        "qr,rjf->jqf", low[:, :adapter_rank_width], gate_up_map, preferred_element_type=jnp.float32
    ).astype(jnp.bfloat16)
    delta_up = jnp.einsum(
        "qr,rjf->jqf", low[:, adapter_rank_width:], up_up_map, preferred_element_type=jnp.float32
    ).astype(jnp.bfloat16)
    got_gate = lax.all_to_all(delta_gate, "gy", split_axis=0, concat_axis=0, tiled=True)
    got_up = lax.all_to_all(delta_up, "gy", split_axis=0, concat_axis=0, tiled=True)
    got_gate = got_gate.reshape(tile_grid_columns * owner_rows, column_count)
    got_up = got_up.reshape(tile_grid_columns * owner_rows, column_count)

    entries = tile_grid_columns * owner_rows
    mine = slot_all // tile_grid_columns == row_gx
    entry = (slot_all % tile_grid_columns) * owner_rows + (lax.iota(jnp.int32, total_rows) // block) * CAP + position
    entry = jnp.where(mine, entry, entries)
    spare_rank = jnp.cumsum(jnp.where(mine, 0, 1)) - 1
    spare_rows = jnp.zeros((entries,), jnp.int32).at[jnp.where(mine, entries, spare_rank)].set(
        lax.iota(jnp.int32, total_rows), mode="drop"
    )
    row_of_entry = spare_rows.at[entry].set(lax.iota(jnp.int32, total_rows), mode="drop")

    gathered = lax.all_gather(tokens, "gy", axis=0, tiled=True)
    row_major = Layout(major_to_minor=(0, 1))
    gate_part = with_layout_constraint(
        jnp.dot(gathered, gate_base_weight, preferred_element_type=jnp.float32).astype(jnp.bfloat16),
        row_major,
    )
    gate_part = gate_part.at[row_of_entry].set(
        (gate_part[row_of_entry].astype(jnp.float32) + got_gate.astype(jnp.float32)).astype(jnp.bfloat16),
        unique_indices=True, mode="promise_in_bounds")
    gate_sum = lax.psum_scatter(gate_part, "gx", scatter_dimension=0, tiled=True).astype(jnp.float32)
    up_part = with_layout_constraint(
        jnp.dot(gathered, up_base_weight, preferred_element_type=jnp.float32).astype(jnp.bfloat16),
        row_major,
    )
    up_part = up_part.at[row_of_entry].set(
        (up_part[row_of_entry].astype(jnp.float32) + got_up.astype(jnp.float32)).astype(jnp.bfloat16),
        unique_indices=True, mode="promise_in_bounds")
    up_sum = lax.psum_scatter(up_part, "gx", scatter_dimension=0, tiled=True).astype(jnp.float32)
    return (jax.nn.silu(gate_sum) * up_sum).astype(jnp.bfloat16)


def solution(mesh):
    return jax.shard_map(
        body,
        mesh=mesh,
        in_specs=(
            P("gy", "gx"),
            P("gx", "gy"),
            P("gx", "gy"),
            P(("gx", "gy"), None, None),
            P(("gx", "gy"), None, None),
            P(),
            P(),
        ),
        out_specs=P("gx", "gy"),
        check_vma=False,
    )
```

```python
import jax
import jax.numpy as jnp
from jax import lax
from jax.sharding import PartitionSpec as P
from jax.experimental.layout import Layout, with_layout_constraint

CAP = 4


def body(
    tokens,
    gate_base_weight,
    up_base_weight,
    adapter_down_maps,
    adapter_up_maps,
    tenant,
    tenant_slot_index,
):
    tile_grid_rows = lax.axis_size("gx")
    tile_grid_columns = lax.axis_size("gy")
    devices = tile_grid_rows * tile_grid_columns
    row_gx = lax.axis_index("gx")
    row_gy = lax.axis_index("gy")
    local_rows = tokens.shape[0]
    tile_width = tokens.shape[1]
    total_rows = tenant.shape[0]
    block = total_rows // tile_grid_rows
    groups = local_rows // block
    tenants = tenant_slot_index.shape[0]
    column_count = gate_base_weight.shape[1]
    doubled_rank = adapter_down_maps.shape[2]
    adapter_rank_width = doubled_rank // 2
    owner_rows = tile_grid_rows * CAP

    slot_all = jnp.sum(
        jnp.where(tenant == lax.iota(jnp.int32, tenants)[None, :], tenant_slot_index[None, :], 0),
        axis=1,
    )
    onehot = (slot_all[:, None] == lax.iota(jnp.int32, devices)[None, :]).astype(jnp.int32)
    blocked = onehot.reshape(tile_grid_rows, block, devices)
    before = jnp.cumsum(blocked, axis=1) - blocked
    position = jnp.sum(before * blocked, axis=2).reshape(total_rows)

    send_slot = lax.dynamic_slice_in_dim(slot_all, row_gy * local_rows, local_rows)
    send_rank = lax.dynamic_slice_in_dim(position, row_gy * local_rows, local_rows)
    target = (send_slot * groups + lax.iota(jnp.int32, local_rows) // block) * CAP + send_rank
    outgoing = jnp.zeros((devices * groups * CAP, tile_width), jnp.bfloat16).at[target].set(tokens)
    arrived = lax.all_to_all(
        outgoing.reshape(devices, groups * CAP, tile_width),
        ("gx", "gy"),
        split_axis=0,
        concat_axis=0,
        tiled=True,
    )
    arrived = arrived.reshape(tile_grid_rows, tile_grid_columns * groups * CAP, tile_width)
    down_local = adapter_down_maps[0].reshape(tile_grid_rows, tile_width, doubled_rank)
    low = jnp.einsum("isk,ikr->sr", arrived, down_local, preferred_element_type=jnp.float32).astype(
        jnp.bfloat16
    )

    gate_up_map = adapter_up_maps[0, :adapter_rank_width].reshape(
        adapter_rank_width, tile_grid_columns, column_count
    )
    up_up_map = adapter_up_maps[0, adapter_rank_width:].reshape(
        adapter_rank_width, tile_grid_columns, column_count
    )
    halves = 2
    half_rows = owner_rows // halves
    got_gate = []
    for h in range(halves):
        piece = jnp.einsum(
            "qr,rjf->jqf", low[h * half_rows:(h + 1) * half_rows, :adapter_rank_width], gate_up_map,
            preferred_element_type=jnp.float32,
        ).astype(jnp.bfloat16)
        got_gate.append(lax.all_to_all(piece, "gy", split_axis=0, concat_axis=0, tiled=True))
    delta_up = jnp.einsum(
        "qr,rjf->jqf", low[:, adapter_rank_width:], up_up_map, preferred_element_type=jnp.float32
    ).astype(jnp.bfloat16)
    got_up = lax.all_to_all(delta_up, "gy", split_axis=0, concat_axis=0, tiled=True)
    got_up = got_up.reshape(tile_grid_columns * owner_rows, column_count)

    entries = tile_grid_columns * owner_rows
    mine = slot_all // tile_grid_columns == row_gx
    row_block = lax.iota(jnp.int32, total_rows) // block
    entry = (slot_all % tile_grid_columns) * owner_rows + row_block * CAP + position
    entry = jnp.where(mine, entry, entries)
    row_of_entry = jnp.zeros((entries,), jnp.int32).at[entry].set(
        lax.iota(jnp.int32, total_rows), mode="drop"
    )
    half_entries = tile_grid_columns * half_rows
    half_rows_of = []
    for h in range(halves):
        in_half = mine & (row_block * CAP // half_rows == h)
        half_entry = (slot_all % tile_grid_columns) * half_rows + row_block * CAP + position - h * half_rows
        half_entry = jnp.where(in_half, half_entry, half_entries)
        half_rows_of.append(
            jnp.zeros((half_entries,), jnp.int32).at[half_entry].set(lax.iota(jnp.int32, total_rows), mode="drop")
        )

    gathered = lax.all_gather(tokens, "gy", axis=0, tiled=True)
    row_major = Layout(major_to_minor=(0, 1))
    gate_part = with_layout_constraint(
        jnp.dot(gathered, gate_base_weight, preferred_element_type=jnp.float32).astype(jnp.bfloat16),
        row_major,
    )
    for h in range(halves):
        gate_part = gate_part.at[half_rows_of[h]].add(got_gate[h].reshape(half_entries, column_count))
    gate_sum = lax.psum_scatter(gate_part, "gx", scatter_dimension=0, tiled=True).astype(jnp.float32)
    up_part = with_layout_constraint(
        jnp.dot(gathered, up_base_weight, preferred_element_type=jnp.float32).astype(jnp.bfloat16),
        row_major,
    )
    up_part = up_part.at[row_of_entry].add(got_up)
    up_sum = lax.psum_scatter(up_part, "gx", scatter_dimension=0, tiled=True).astype(jnp.float32)
    return (jax.nn.silu(gate_sum) * up_sum).astype(jnp.bfloat16)


def solution(mesh):
    return jax.shard_map(
        body,
        mesh=mesh,
        in_specs=(
            P("gy", "gx"),
            P("gx", "gy"),
            P("gx", "gy"),
            P(("gx", "gy"), None, None),
            P(("gx", "gy"), None, None),
            P(),
            P(),
        ),
        out_specs=P("gx", "gy"),
        check_vma=False,
    )
```

```python
import jax
import jax.numpy as jnp
from jax import lax
from jax.sharding import PartitionSpec as P
from jax.experimental.layout import Layout, with_layout_constraint

CAP = 4


def body(
    tokens,
    gate_base_weight,
    up_base_weight,
    adapter_down_maps,
    adapter_up_maps,
    tenant,
    tenant_slot_index,
):
    tile_grid_rows = lax.axis_size("gx")
    tile_grid_columns = lax.axis_size("gy")
    devices = tile_grid_rows * tile_grid_columns
    row_gx = lax.axis_index("gx")
    row_gy = lax.axis_index("gy")
    local_rows = tokens.shape[0]
    tile_width = tokens.shape[1]
    total_rows = tenant.shape[0]
    block = total_rows // tile_grid_rows
    groups = local_rows // block
    tenants = tenant_slot_index.shape[0]
    column_count = gate_base_weight.shape[1]
    doubled_rank = adapter_down_maps.shape[2]
    adapter_rank_width = doubled_rank // 2
    owner_rows = tile_grid_rows * CAP

    slot_all = jnp.sum(
        jnp.where(tenant == lax.iota(jnp.int32, tenants)[None, :], tenant_slot_index[None, :], 0),
        axis=1,
    )
    onehot = (slot_all[:, None] == lax.iota(jnp.int32, devices)[None, :]).astype(jnp.int32)
    blocked = onehot.reshape(tile_grid_rows, block, devices)
    before = jnp.cumsum(blocked, axis=1) - blocked
    position = jnp.sum(before * blocked, axis=2).reshape(total_rows)

    send_slot = lax.dynamic_slice_in_dim(slot_all, row_gy * local_rows, local_rows)
    send_rank = lax.dynamic_slice_in_dim(position, row_gy * local_rows, local_rows)
    target = (send_slot * groups + lax.iota(jnp.int32, local_rows) // block) * CAP + send_rank
    chosen = (target[None, :] == lax.iota(jnp.int32, devices * groups * CAP)[:, None]).astype(jnp.bfloat16)
    outgoing = jnp.dot(chosen, tokens, preferred_element_type=jnp.float32).astype(jnp.bfloat16)
    arrived = lax.all_to_all(
        outgoing.reshape(devices, groups * CAP, tile_width),
        ("gx", "gy"),
        split_axis=0,
        concat_axis=0,
        tiled=True,
    )
    arrived = arrived.reshape(tile_grid_rows, tile_grid_columns * groups * CAP, tile_width)
    down_local = adapter_down_maps[0].reshape(tile_grid_rows, tile_width, doubled_rank)
    low = jnp.einsum("isk,ikr->sr", arrived, down_local, preferred_element_type=jnp.float32).astype(
        jnp.bfloat16
    )

    gate_up_map = adapter_up_maps[0, :adapter_rank_width].reshape(
        adapter_rank_width, tile_grid_columns, column_count
    )
    up_up_map = adapter_up_maps[0, adapter_rank_width:].reshape(
        adapter_rank_width, tile_grid_columns, column_count
    )
    delta_gate = jnp.einsum(
        "qr,rjf->jqf", low[:, :adapter_rank_width], gate_up_map, preferred_element_type=jnp.float32
    ).astype(jnp.bfloat16)
    delta_up = jnp.einsum(
        "qr,rjf->jqf", low[:, adapter_rank_width:], up_up_map, preferred_element_type=jnp.float32
    ).astype(jnp.bfloat16)
    got_gate = lax.all_to_all(delta_gate, "gy", split_axis=0, concat_axis=0, tiled=True)
    got_up = lax.all_to_all(delta_up, "gy", split_axis=0, concat_axis=0, tiled=True)
    got_gate = got_gate.reshape(tile_grid_columns * owner_rows, column_count)
    got_up = got_up.reshape(tile_grid_columns * owner_rows, column_count)

    entries = tile_grid_columns * owner_rows
    mine = slot_all // tile_grid_columns == row_gx
    entry = (slot_all % tile_grid_columns) * owner_rows + (lax.iota(jnp.int32, total_rows) // block) * CAP + position
    entry = jnp.where(mine, entry, entries)
    row_of_entry = jnp.zeros((entries,), jnp.int32).at[entry].set(
        lax.iota(jnp.int32, total_rows), mode="drop"
    )

    gathered = lax.all_gather(tokens, "gy", axis=0, tiled=True)
    row_major = Layout(major_to_minor=(0, 1))
    gate_part = with_layout_constraint(
        jnp.dot(gathered, gate_base_weight, preferred_element_type=jnp.float32).astype(jnp.bfloat16),
        row_major,
    )
    gate_part = gate_part.at[row_of_entry].add(got_gate)
    gate_sum = lax.psum_scatter(gate_part, "gx", scatter_dimension=0, tiled=True).astype(jnp.float32)
    up_part = with_layout_constraint(
        jnp.dot(gathered, up_base_weight, preferred_element_type=jnp.float32).astype(jnp.bfloat16),
        row_major,
    )
    up_part = up_part.at[row_of_entry].add(got_up)
    up_sum = lax.psum_scatter(up_part, "gx", scatter_dimension=0, tiled=True).astype(jnp.float32)
    return (jax.nn.silu(gate_sum) * up_sum).astype(jnp.bfloat16)


def solution(mesh):
    return jax.shard_map(
        body,
        mesh=mesh,
        in_specs=(
            P("gy", "gx"),
            P("gx", "gy"),
            P("gx", "gy"),
            P(("gx", "gy"), None, None),
            P(("gx", "gy"), None, None),
            P(),
            P(),
        ),
        out_specs=P("gx", "gy"),
        check_vma=False,
    )
```

```python
import jax
import jax.numpy as jnp
from jax import lax
from jax.sharding import PartitionSpec as P
from jax.experimental.layout import Layout, with_layout_constraint

CAP = 4


def body(
    tokens,
    gate_base_weight,
    up_base_weight,
    adapter_down_maps,
    adapter_up_maps,
    tenant,
    tenant_slot_index,
):
    tile_grid_rows = lax.axis_size("gx")
    tile_grid_columns = lax.axis_size("gy")
    devices = tile_grid_rows * tile_grid_columns
    row_gx = lax.axis_index("gx")
    row_gy = lax.axis_index("gy")
    local_rows = tokens.shape[0]
    tile_width = tokens.shape[1]
    total_rows = tenant.shape[0]
    block = total_rows // tile_grid_rows
    groups = local_rows // block
    tenants = tenant_slot_index.shape[0]
    column_count = gate_base_weight.shape[1]
    doubled_rank = adapter_down_maps.shape[2]
    adapter_rank_width = doubled_rank // 2
    owner_rows = tile_grid_rows * CAP

    slot_all = jnp.sum(
        jnp.where(tenant == lax.iota(jnp.int32, tenants)[None, :], tenant_slot_index[None, :], 0),
        axis=1,
    )
    by_block = slot_all.reshape(tile_grid_rows, block)
    earlier = lax.iota(jnp.int32, block)[None, :] < lax.iota(jnp.int32, block)[:, None]
    same = (by_block[:, :, None] == by_block[:, None, :]) & earlier[None, :, :]
    position = jnp.sum(same.astype(jnp.int32), axis=2).reshape(total_rows)

    send_slot = lax.dynamic_slice_in_dim(slot_all, row_gy * local_rows, local_rows)
    send_rank = lax.dynamic_slice_in_dim(position, row_gy * local_rows, local_rows)
    target = (send_slot * groups + lax.iota(jnp.int32, local_rows) // block) * CAP + send_rank
    chosen = (target[None, :] == lax.iota(jnp.int32, devices * groups * CAP)[:, None]).astype(jnp.bfloat16)
    outgoing = jnp.dot(chosen, tokens, preferred_element_type=jnp.float32).astype(jnp.bfloat16)
    arrived = lax.all_to_all(
        outgoing.reshape(devices, groups * CAP, tile_width),
        ("gx", "gy"),
        split_axis=0,
        concat_axis=0,
        tiled=True,
    )
    arrived = arrived.reshape(tile_grid_rows, tile_grid_columns * groups * CAP, tile_width)
    down_local = adapter_down_maps[0].reshape(tile_grid_rows, tile_width, doubled_rank)
    low = jnp.einsum("isk,ikr->sr", arrived, down_local, preferred_element_type=jnp.float32).astype(
        jnp.bfloat16
    )

    gate_up_map = adapter_up_maps[0, :adapter_rank_width].reshape(
        adapter_rank_width, tile_grid_columns, column_count
    )
    up_up_map = adapter_up_maps[0, adapter_rank_width:].reshape(
        adapter_rank_width, tile_grid_columns, column_count
    )
    delta_gate = jnp.einsum(
        "qr,rjf->jqf", low[:, :adapter_rank_width], gate_up_map, preferred_element_type=jnp.float32
    ).astype(jnp.bfloat16)
    delta_up = jnp.einsum(
        "qr,rjf->jqf", low[:, adapter_rank_width:], up_up_map, preferred_element_type=jnp.float32
    ).astype(jnp.bfloat16)
    got_gate = lax.all_to_all(delta_gate, "gy", split_axis=0, concat_axis=0, tiled=True)
    got_up = lax.all_to_all(delta_up, "gy", split_axis=0, concat_axis=0, tiled=True)
    got_gate = got_gate.reshape(tile_grid_columns * owner_rows, column_count)
    got_up = got_up.reshape(tile_grid_columns * owner_rows, column_count)

    entries = tile_grid_columns * owner_rows
    mine = slot_all // tile_grid_columns == row_gx
    entry = (slot_all % tile_grid_columns) * owner_rows + (lax.iota(jnp.int32, total_rows) // block) * CAP + position
    entry = jnp.where(mine, entry, entries)
    row_of_entry = jnp.zeros((entries,), jnp.int32).at[entry].set(
        lax.iota(jnp.int32, total_rows), mode="drop"
    )

    gathered = lax.all_gather(tokens, "gy", axis=0, tiled=True)
    row_major = Layout(major_to_minor=(0, 1))
    gate_part = with_layout_constraint(
        jnp.dot(gathered, gate_base_weight, preferred_element_type=jnp.float32).astype(jnp.bfloat16),
        row_major,
    )
    gate_part = gate_part.at[row_of_entry].add(got_gate)
    gate_sum = lax.psum_scatter(gate_part, "gx", scatter_dimension=0, tiled=True).astype(jnp.float32)
    up_part = with_layout_constraint(
        jnp.dot(gathered, up_base_weight, preferred_element_type=jnp.float32).astype(jnp.bfloat16),
        row_major,
    )
    up_part = up_part.at[row_of_entry].add(got_up)
    up_sum = lax.psum_scatter(up_part, "gx", scatter_dimension=0, tiled=True).astype(jnp.float32)
    return (jax.nn.silu(gate_sum) * up_sum).astype(jnp.bfloat16)


def solution(mesh):
    return jax.shard_map(
        body,
        mesh=mesh,
        in_specs=(
            P("gy", "gx"),
            P("gx", "gy"),
            P("gx", "gy"),
            P(("gx", "gy"), None, None),
            P(("gx", "gy"), None, None),
            P(),
            P(),
        ),
        out_specs=P("gx", "gy"),
        check_vma=False,
    )
```

```python
import jax
import jax.numpy as jnp
from jax import lax
from jax.sharding import PartitionSpec as P
from jax.experimental.layout import Layout, with_layout_constraint

CAP = 4


def body(
    tokens,
    gate_base_weight,
    up_base_weight,
    adapter_down_maps,
    adapter_up_maps,
    tenant,
    tenant_slot_index,
):
    tile_grid_rows = lax.axis_size("gx")
    tile_grid_columns = lax.axis_size("gy")
    devices = tile_grid_rows * tile_grid_columns
    row_gx = lax.axis_index("gx")
    row_gy = lax.axis_index("gy")
    local_rows = tokens.shape[0]
    tile_width = tokens.shape[1]
    total_rows = tenant.shape[0]
    block = total_rows // tile_grid_rows
    groups = local_rows // block
    tenants = tenant_slot_index.shape[0]
    column_count = gate_base_weight.shape[1]
    doubled_rank = adapter_down_maps.shape[2]
    adapter_rank_width = doubled_rank // 2
    owner_rows = tile_grid_rows * CAP

    slot_all = jnp.take(tenant_slot_index, tenant[:, 0], axis=0, mode="clip")
    by_block = slot_all.reshape(tile_grid_rows, block)
    earlier = lax.iota(jnp.int32, block)[None, :] < lax.iota(jnp.int32, block)[:, None]
    same = (by_block[:, :, None] == by_block[:, None, :]) & earlier[None, :, :]
    position = jnp.sum(same.astype(jnp.int32), axis=2).reshape(total_rows)

    send_slot = lax.dynamic_slice_in_dim(slot_all, row_gy * local_rows, local_rows)
    send_rank = lax.dynamic_slice_in_dim(position, row_gy * local_rows, local_rows)
    target = (send_slot * groups + lax.iota(jnp.int32, local_rows) // block) * CAP + send_rank
    chosen = (target[None, :] == lax.iota(jnp.int32, devices * groups * CAP)[:, None]).astype(jnp.bfloat16)
    outgoing = jnp.dot(chosen, tokens, preferred_element_type=jnp.float32).astype(jnp.bfloat16)
    arrived = lax.all_to_all(
        outgoing.reshape(devices, groups * CAP, tile_width),
        ("gx", "gy"),
        split_axis=0,
        concat_axis=0,
        tiled=True,
    )
    arrived = arrived.reshape(tile_grid_rows, tile_grid_columns * groups * CAP, tile_width)
    down_local = adapter_down_maps[0].reshape(tile_grid_rows, tile_width, doubled_rank)
    low = jnp.einsum("isk,ikr->sr", arrived, down_local, preferred_element_type=jnp.float32).astype(
        jnp.bfloat16
    )

    gate_up_map = adapter_up_maps[0, :adapter_rank_width].reshape(
        adapter_rank_width, tile_grid_columns, column_count
    )
    up_up_map = adapter_up_maps[0, adapter_rank_width:].reshape(
        adapter_rank_width, tile_grid_columns, column_count
    )
    delta_gate = jnp.einsum(
        "qr,rjf->jqf", low[:, :adapter_rank_width], gate_up_map, preferred_element_type=jnp.float32
    ).astype(jnp.bfloat16)
    delta_up = jnp.einsum(
        "qr,rjf->jqf", low[:, adapter_rank_width:], up_up_map, preferred_element_type=jnp.float32
    ).astype(jnp.bfloat16)
    got_gate = lax.all_to_all(delta_gate, "gy", split_axis=0, concat_axis=0, tiled=True)
    got_up = lax.all_to_all(delta_up, "gy", split_axis=0, concat_axis=0, tiled=True)
    got_gate = got_gate.reshape(tile_grid_columns * owner_rows, column_count)
    got_up = got_up.reshape(tile_grid_columns * owner_rows, column_count)

    entries = tile_grid_columns * owner_rows
    mine = slot_all // tile_grid_columns == row_gx
    entry = (slot_all % tile_grid_columns) * owner_rows + (lax.iota(jnp.int32, total_rows) // block) * CAP + position
    entry = jnp.where(mine, entry, entries)
    row_of_entry = jnp.zeros((entries,), jnp.int32).at[entry].set(
        lax.iota(jnp.int32, total_rows), mode="drop"
    )

    gathered = lax.all_gather(tokens, "gy", axis=0, tiled=True)
    row_major = Layout(major_to_minor=(0, 1))
    gate_part = with_layout_constraint(
        jnp.dot(gathered, gate_base_weight, preferred_element_type=jnp.float32).astype(jnp.bfloat16),
        row_major,
    )
    gate_part = gate_part.at[row_of_entry].add(got_gate)
    gate_sum = lax.psum_scatter(gate_part, "gx", scatter_dimension=0, tiled=True).astype(jnp.float32)
    up_part = with_layout_constraint(
        jnp.dot(gathered, up_base_weight, preferred_element_type=jnp.float32).astype(jnp.bfloat16),
        row_major,
    )
    up_part = up_part.at[row_of_entry].add(got_up)
    up_sum = lax.psum_scatter(up_part, "gx", scatter_dimension=0, tiled=True).astype(jnp.float32)
    return (jax.nn.silu(gate_sum) * up_sum).astype(jnp.bfloat16)


def solution(mesh):
    return jax.shard_map(
        body,
        mesh=mesh,
        in_specs=(
            P("gy", "gx"),
            P("gx", "gy"),
            P("gx", "gy"),
            P(("gx", "gy"), None, None),
            P(("gx", "gy"), None, None),
            P(),
            P(),
        ),
        out_specs=P("gx", "gy"),
        check_vma=False,
    )
```
